128 devices in a mesh: dp: 16 (over x, y), expert: 8 (over z, core).
Axes of the slice: x: 4, y: 4, z: 4, core: 2. Of those that a mesh axis runs over, the one named last changes fastest.
Arguments:
- frames: bfloat16 [65536, 1024], P(('dp', 'expert')), may hold values from -6 to 6
- lengths: int32 [256], P(('dp', 'expert')), may hold values from 64 to 256, as said below
- expert_ids: int32 [65536, 1], P(('dp', 'expert')), may hold values from 0 to 7; in each aligned block of 512 rows (0 to 511, 512 to 1023, ...) at most 72 rows name the same one
- conv_kernel: float32 [31, 1024], replicated, may hold values from -1 to 1
- conv_gain: float32 [1024], replicated, may hold values from 0.25 to 1.75
- ffn_gain: float32 [1024], replicated, may hold values from 0.25 to 1.75
- w_in: bfloat16 [8, 1024, 4096], P('expert'), may hold values from -0.1875 to 0.1875
- w_out: bfloat16 [8, 4096, 1024], P('expert'), may hold values from -0.09375 to 0.09375
- out_grad: bfloat16 [65536, 1024], P(('dp', 'expert')), may hold values from -6 to 6
Outputs:
- block_out: bfloat16 [65536, 1024], P(('dp', 'expert'))
- frames_grad: bfloat16 [65536, 1024], P(('dp', 'expert'))
- w_in_grad: float32 [8, 1024, 4096], P('expert', None, 'dp')
- w_out_grad: float32 [8, 4096, 1024], P('expert', 'dp')
- kernel_grad: float32 [31, 1024], replicated
- gain_grads: float32 [2, 1024], replicated
The draws below stay inside these ranges and needn't reach their ends.
Inputs may be any that keep to these rules, and one draw needn't show every extreme that they name: `expert_ids`: in the rows of one device (aligned blocks of 512 rows) no expert is named more than 72 times, a bound that some block reaches. `lengths`: all utterances of some device have 256 live frames.
All inputs are finite; a program needn't handle non-finite values.
Results may differ from the reference program's by a relative error of at most 0.0053.
Values may be sent and summed in bfloat16 or wider, within the bound.
No kernel may reach another device: no remote copies, remote signals or barrier semaphores. Data moves between devices by JAX's collectives and lax.ppermute only.
A program may use at most 256 MiB of HBM per device.

```python
import math
import jax
import jax.numpy as jnp
import numpy as np
from jax import lax

D = 1024
FF = 4096
KS = 31
UTT_LEN = 256
UTT_DEV = 2
EXPERTS = 8
CAP = 72
UTTS = 256
FRAMES = 65536
N_DP = 16
N_EXPERT = 8


def draw_lengths(key, part):
    key_len, key_owner = jax.random.split(key)
    base_len = jax.random.randint(key_len, (UTTS,), UTT_LEN // 4, UTT_LEN + 1)
    owner_block = jax.random.randint(key_owner, (), 0, UTTS // UTT_DEV)
    block_of = jnp.arange(UTTS) // UTT_DEV
    return jnp.where(block_of == owner_block, UTT_LEN, base_len).astype(jnp.int32)


def block_scale(own_key, shape, cuts, low, top_value):
    gain = 1.0
    for dim, blocks in cuts:
        draws = jax.random.uniform(jax.random.fold_in(jax.random.fold_in(own_key, 6), dim), (blocks,), jnp.float32, low / len(cuts), top_value / len(cuts))
        gain = gain * jnp.repeat(jnp.exp(draws), shape[dim] // blocks).reshape((-1,) + (1,) * (len(shape) - 1 - dim))
    return gain


def shared_out(stream_key, own, number, rows, count, top, most, slope):
    ranking = jax.random.permutation(stream_key, count)
    crowded, usual = shares(count, rows * top, most, slope, True), shares(count, rows * top, most, slope, False)
    places = jnp.arange(count)

    def named(sizes, offset_by):
        used = int((sizes > 0).sum())
        fixed = max(1, used // 4)
        passed = fixed + (places - fixed + offset_by * (used - fixed)) % max(1, count - fixed)
        return jnp.zeros((count,), jnp.int32).at[ranking[jnp.where(places < fixed, places, passed)]].set(jnp.asarray(sizes, jnp.int32))

    sizes = jnp.where(number % 4 == 0, named(crowded, number // 4), named(usual, number - number // 4 - 1))
    mixed = jax.random.permutation(jax.random.fold_in(own, 3), count)
    donor, sink = mixed[0:count // 2 * 2:2], mixed[1:count // 2 * 2:2]
    room = jnp.minimum(sizes[donor] - 1, most - sizes[sink]) // 2
    room = jnp.where((donor == ranking[0]) | (sink == ranking[0]) | (sizes[sink] == 0), 0, jnp.maximum(room, 0))
    passed = jax.random.randint(jax.random.fold_in(own, 4), (count // 2,), 0, 1 << 20) % (room + 1)
    sizes = sizes.at[donor].add(-passed).at[sink].add(passed)
    items = jnp.searchsorted(jnp.cumsum(sizes), jnp.arange(rows * top), side="right").astype(jnp.int32)
    listing = items.reshape(top, rows).T
    listing = listing[jax.random.permutation(jax.random.fold_in(own, 1), rows)]
    offset_by = jax.random.randint(jax.random.fold_in(own, 2), (rows, 1), 0, top)
    return jnp.take_along_axis(listing, (jnp.arange(top)[None, :] + offset_by) % top, axis=1)


def shares(number_of, total, reach, slope, full):
    portions = [(1 << 20) // math.isqrt(grade ** slope) + 1 for grade in range(1, number_of + 1)]
    largest = reach if full else min(reach, max(-(-total // number_of), total * portions[0] // sum(portions)))
    least = 1 if total - largest >= number_of - 1 else 0
    given, surplus = [largest] + [least] * (number_of - 1), total - largest - least * (number_of - 1)
    while surplus > 0:
        movable = [i for i in range(1, number_of) if given[i] < largest] or [i for i in range(1, number_of) if given[i] < reach]
        whole, remaining = sum([portions[i] for i in movable]), surplus
        for i in movable:
            addition = min(reach - given[i], max(1, remaining * portions[i] // whole), surplus)
            given[i] = given[i] + addition
            surplus = surplus - addition
    return np.array(given)


def noise(key, extent, deviation, most, cuts=(), held_as=jnp.bfloat16):
    drawn = jax.random.normal(key, extent, jnp.float32) * deviation
    if len(cuts) > 0:
        drawn = block_scale(key, extent, cuts, -0.22, 0.18) * drawn
    return jnp.clip(drawn, min=-most, max=most).astype(held_as)


def setup_inputs(seed: int = 0) -> dict:
    key_of = jax.random.split(jax.random.key(seed), 10)
    frames = noise(key_of[0], (FRAMES, D), 1.0, 6.0, ((0, 128),))
    lengths = draw_lengths(jax.random.fold_in(key_of[9], 71), 0)
    expert_ids_keys = jax.random.split(jax.random.fold_in(key_of[2], 1), FRAMES // (UTT_DEV * UTT_LEN))
    expert_ids_turns = jax.random.permutation(jax.random.fold_in(key_of[2], 3), FRAMES // (UTT_DEV * UTT_LEN))
    expert_ids = jax.vmap(lambda own, number: shared_out(jax.random.fold_in(key_of[2], 2), own, number, UTT_DEV * UTT_LEN, EXPERTS, 1, CAP, 2))(expert_ids_keys, expert_ids_turns).reshape((FRAMES, 1))
    conv_kernel = noise(key_of[3], (KS, D), KS ** -0.5, 1.0, (), jnp.float32)
    conv_gain = jnp.clip(1.0 + 0.15 * jax.random.normal(key_of[4], (D,), jnp.float32), 0.25, 1.75)
    ffn_gain = jnp.clip(1.0 + 0.15 * jax.random.normal(key_of[5], (D,), jnp.float32), 0.25, 1.75)
    w_in = noise(key_of[6], (EXPERTS, D, FF), D ** -0.5, 0.1875, ((0, 8),))
    w_out = noise(key_of[7], (EXPERTS, FF, D), FF ** -0.5, 0.09375, ((0, 8),))
    out_grad = noise(key_of[8], (FRAMES, D), 1.0, 6.0, ((0, 128),))
    return dict(frames=frames, lengths=lengths, expert_ids=expert_ids, conv_kernel=conv_kernel, conv_gain=conv_gain, ffn_gain=ffn_gain, w_in=w_in, w_out=w_out, out_grad=out_grad)


def layer_norm(values, gain_vec):
    row_mean = lax.optimization_barrier(jnp.mean(values, axis=-1, keepdims=True))
    centered = values - row_mean
    row_var = lax.optimization_barrier(jnp.mean(centered * centered, axis=-1, keepdims=True))
    return centered * lax.rsqrt(row_var + 1e-05) * gain_vec

def conv_module(frames_f, live_mask, conv_kernel, conv_gain, ffn_gain):
    normed_conv = layer_norm(frames_f, conv_gain) * live_mask
    tap_count = conv_kernel.shape[0]
    half_span = (tap_count - 1) // 2
    utt_len = frames_f.shape[1]
    padded = jnp.pad(normed_conv, ((0, 0), (half_span, half_span), (0, 0)))
    conv_out = jnp.zeros_like(normed_conv)
    for tap_index in range(tap_count):
        conv_out = conv_out + conv_kernel[tap_index] * padded[:, tap_index:tap_index + utt_len]
    residual = frames_f + live_mask * jax.nn.silu(conv_out)
    return (residual, layer_norm(residual, ffn_gain))

def silu_slope(values):
    sig_val = jax.nn.sigmoid(values)
    return sig_val * (1.0 + values * (1.0 - sig_val))

def expert_pass(item):
    weights_in, weights_out, rows_in, rows_grad = item
    pre_act = jnp.dot(rows_in, weights_in, preferred_element_type=jnp.float32)
    hidden = jax.nn.silu(pre_act).astype(jnp.bfloat16)
    out_rows = jnp.dot(hidden, weights_out, preferred_element_type=jnp.float32).astype(jnp.bfloat16)
    hidden_grad = jnp.dot(rows_grad, weights_out.T, preferred_element_type=jnp.float32)
    pre_grad = (hidden_grad * silu_slope(pre_act)).astype(jnp.bfloat16)
    back_rows = jnp.dot(pre_grad, weights_in.T, preferred_element_type=jnp.float32).astype(jnp.bfloat16)
    grad_in = jnp.dot(rows_in.T, pre_grad, preferred_element_type=jnp.float32)
    grad_out = jnp.dot(hidden.T, rows_grad, preferred_element_type=jnp.float32)
    return (out_rows, back_rows, grad_in, grad_out)

def reference(frames, lengths, expert_ids, conv_kernel, conv_gain, ffn_gain, w_in, w_out, out_grad):
    block_count = UTTS // UTT_DEV
    live_mask = (jnp.arange(UTT_LEN, dtype=jnp.int32)[None, :] < lengths[:, None]).astype(jnp.float32)[:, :, None]
    frames_f = frames.astype(jnp.float32).reshape(block_count, UTT_DEV, UTT_LEN, D)
    mask_blocks = live_mask.reshape(block_count, UTT_DEV, UTT_LEN, 1)

    def forward_block(item):
        return conv_module(item[0], item[1], conv_kernel, conv_gain, ffn_gain)
    residual, normed = lax.map(forward_block, (frames_f, mask_blocks))
    residual = residual.reshape(FRAMES, D)
    expert_in = normed.reshape(FRAMES, D).astype(jnp.bfloat16)
    live_flat = live_mask.reshape(FRAMES) > 0.5
    slot_count = N_DP * N_EXPERT * CAP
    target = jnp.where(live_flat, expert_ids[:, 0], EXPERTS).astype(jnp.int32)
    one_hot = (target[:, None] == jnp.arange(EXPERTS, dtype=jnp.int32)[None, :]).astype(jnp.int32)
    rank_in = lax.optimization_barrier(jnp.sum((jnp.cumsum(one_hot, axis=0, dtype=jnp.int32) - 1) * one_hot, axis=1)).astype(jnp.int32)
    dest_slot = jnp.where(live_flat, target * slot_count + rank_in, EXPERTS * slot_count).astype(jnp.int32)
    routed_grad = jnp.where(live_flat[:, None], out_grad, jnp.zeros_like(out_grad))
    buffer_in = jnp.zeros((EXPERTS * slot_count, D), jnp.bfloat16).at[dest_slot].set(expert_in, mode='drop')
    buffer_grad = jnp.zeros((EXPERTS * slot_count, D), jnp.bfloat16).at[dest_slot].set(routed_grad, mode='drop')
    outs_all, backs_all, w_in_grad, w_out_grad = lax.map(expert_pass, (w_in, w_out, buffer_in.reshape(EXPERTS, slot_count, D), buffer_grad.reshape(EXPERTS, slot_count, D)))
    safe_slot = jnp.minimum(dest_slot, EXPERTS * slot_count - 1).astype(jnp.int32)
    zero_rows = jnp.zeros((FRAMES, D), jnp.float32)
    expert_out = jnp.where(live_flat[:, None], outs_all.reshape(EXPERTS * slot_count, D)[safe_slot].astype(jnp.float32), zero_rows)
    expert_back = jnp.where(live_flat[:, None], backs_all.reshape(EXPERTS * slot_count, D)[safe_slot].astype(jnp.float32), zero_rows)
    block_out = (residual + expert_out).astype(jnp.bfloat16)
    grad_blocks = out_grad.astype(jnp.float32).reshape(block_count, UTT_DEV, UTT_LEN, D)
    back_blocks = expert_back.reshape(block_count, UTT_DEV, UTT_LEN, D)

    def backward_block(item):
        block_frames, block_mask, block_grad, block_back = item

        def local_map(frames_in, kernel_in, gain_conv, gain_ffn):
            return conv_module(frames_in, block_mask, kernel_in, gain_conv, gain_ffn)
        unused_out, pull_back = jax.vjp(local_map, block_frames, conv_kernel, conv_gain, ffn_gain)
        return pull_back((block_grad, block_back))
    frames_grad, kernel_parts, conv_parts, ffn_parts = lax.map(backward_block, (frames_f, mask_blocks, grad_blocks, back_blocks))
    kernel_grad = lax.optimization_barrier(jnp.sum(kernel_parts, axis=0))
    gain_grads = jnp.stack([lax.optimization_barrier(jnp.sum(conv_parts, axis=0)), lax.optimization_barrier(jnp.sum(ffn_parts, axis=0))])
    return (block_out, frames_grad.reshape(FRAMES, D).astype(jnp.bfloat16), w_in_grad, w_out_grad, kernel_grad, gain_grads)
```

```python
import jax
import jax.numpy as jnp
from jax import lax
from jax.sharding import PartitionSpec as P


def layer_norm(values, gain_vec):
    row_mean = jnp.mean(values, axis=-1, keepdims=True)
    centered = values - row_mean
    row_var = jnp.mean(centered * centered, axis=-1, keepdims=True)
    return centered * lax.rsqrt(row_var + 1e-05) * gain_vec


def conv_module(frames_f, live_mask, conv_kernel, conv_gain, ffn_gain):
    normed_conv = layer_norm(frames_f, conv_gain) * live_mask
    tap_count = conv_kernel.shape[0]
    half_span = (tap_count - 1) // 2
    utt_len = frames_f.shape[1]
    padded = jnp.pad(normed_conv, ((0, 0), (half_span, half_span), (0, 0)))
    conv_out = jnp.zeros_like(normed_conv)
    for tap_index in range(tap_count):
        conv_out = conv_out + conv_kernel[tap_index] * padded[:, tap_index : tap_index + utt_len]
    residual = frames_f + live_mask * jax.nn.silu(conv_out)
    return (residual, layer_norm(residual, ffn_gain))


def silu_slope(values):
    sig_val = jax.nn.sigmoid(values)
    return sig_val * (1.0 + values * (1.0 - sig_val))


def contract_rows(left_rows, right_rows):
    return lax.dot_general(
        left_rows, right_rows, (((0,), (0,)), ((), ())), preferred_element_type=jnp.float32
    )


def times_transpose(left_rows, matrix):
    return lax.dot_general(
        left_rows, matrix, (((1,), (1,)), ((), ())), preferred_element_type=jnp.float32
    )


def butterfly_sum(values, axis_names):
    for axis_name in axis_names:
        axis_len = lax.axis_size(axis_name)
        step = 1
        while step < axis_len:
            pairs = [(i, i ^ step) for i in range(axis_len)]
            values = values + lax.ppermute(values, axis_name, pairs)
            step *= 2
    return values


def shards(frames, lengths, expert_ids, conv_kernel, conv_gain, ffn_gain, w_in, w_out, out_grad):
    utt_count = lengths.shape[0]
    frame_count = frames.shape[0]
    utt_len = frame_count // utt_count
    feat_width = frames.shape[1]
    expert_count = lax.axis_size("expert")
    capacity = max(8, 8 * (9 * frame_count // (64 * expert_count)))
    slot_total = expert_count * capacity
    live_mask = (jnp.arange(utt_len, dtype=jnp.int32)[None, :] < lengths[:, None]).astype(
        jnp.float32
    )[:, :, None]
    frames_f = frames.astype(jnp.float32).reshape(utt_count, utt_len, feat_width)
    residual, normed = conv_module(frames_f, live_mask, conv_kernel, conv_gain, ffn_gain)
    expert_in = normed.reshape(frame_count, feat_width).astype(jnp.bfloat16)
    live_flat = live_mask.reshape(frame_count) > 0.5
    target = jnp.where(live_flat, expert_ids[:, 0], expert_count)
    one_hot = (target[:, None] == jnp.arange(expert_count, dtype=jnp.int32)[None, :]).astype(
        jnp.int32
    )
    rank_in = jnp.sum((jnp.cumsum(one_hot, axis=0, dtype=jnp.int32) - 1) * one_hot, axis=1)
    dest_slot = jnp.where(live_flat, target * capacity + rank_in, slot_total)
    routed_grad = jnp.where(live_flat[:, None], out_grad, jnp.zeros_like(out_grad))
    send_in = (
        jnp.zeros((slot_total, feat_width), jnp.bfloat16).at[dest_slot].set(expert_in, mode="drop")
    )
    send_grad = (
        jnp.zeros((slot_total, feat_width), jnp.bfloat16)
        .at[dest_slot]
        .set(routed_grad, mode="drop")
    )
    recv_in, recv_grad = (
        lax.all_to_all(
            send_in.reshape(expert_count, capacity, feat_width),
            "expert",
            split_axis=0,
            concat_axis=0,
            tiled=True,
        ),
        lax.all_to_all(
            send_grad.reshape(expert_count, capacity, feat_width),
            "expert",
            split_axis=0,
            concat_axis=0,
            tiled=True,
        ),
    )
    routed_in = recv_in.reshape(slot_total, feat_width)
    grad_rows = recv_grad.reshape(slot_total, feat_width)
    weights_in = w_in[0]
    weights_out = w_out[0]
    pre_act = jnp.dot(routed_in, weights_in, preferred_element_type=jnp.float32)
    hidden = jax.nn.silu(pre_act).astype(jnp.bfloat16)
    full_out = contract_rows(hidden, grad_rows)
    full_out, pre_act, hidden, grad_rows, routed_in = lax.optimization_barrier(
        (full_out, pre_act, hidden, grad_rows, routed_in)
    )
    grad_out = lax.psum_scatter(full_out, "dp", scatter_dimension=0, tiled=True)
    out_rows = jnp.dot(hidden, weights_out, preferred_element_type=jnp.float32).astype(jnp.bfloat16)
    hidden_grad = times_transpose(grad_rows, weights_out)
    pre_grad = (hidden_grad * silu_slope(pre_act)).astype(jnp.bfloat16)
    full_in = contract_rows(routed_in, pre_grad)
    full_in, out_rows, pre_grad = lax.optimization_barrier((full_in, out_rows, pre_grad))
    grad_in = lax.psum_scatter(full_in, "dp", scatter_dimension=1, tiled=True)
    back_rows = times_transpose(pre_grad, weights_in).astype(jnp.bfloat16)
    ret_out, ret_back = (
        lax.all_to_all(
            out_rows.reshape(expert_count, capacity, feat_width),
            "expert",
            split_axis=0,
            concat_axis=0,
            tiled=True,
        ),
        lax.all_to_all(
            back_rows.reshape(expert_count, capacity, feat_width),
            "expert",
            split_axis=0,
            concat_axis=0,
            tiled=True,
        ),
    )
    safe_slot = jnp.minimum(dest_slot, slot_total - 1)
    zero_rows = jnp.zeros((frame_count, feat_width), jnp.float32)
    expert_out = jnp.where(
        live_flat[:, None],
        ret_out.reshape(slot_total, feat_width)[safe_slot].astype(jnp.float32),
        zero_rows,
    )
    expert_back = jnp.where(
        live_flat[:, None],
        ret_back.reshape(slot_total, feat_width)[safe_slot].astype(jnp.float32),
        zero_rows,
    )
    block_out = (residual.reshape(frame_count, feat_width) + expert_out).astype(jnp.bfloat16)

    def local_map(frames_in, kernel_in, gain_conv, gain_ffn):
        return conv_module(frames_in, live_mask, kernel_in, gain_conv, gain_ffn)

    unused_out, pull_back = jax.vjp(local_map, frames_f, conv_kernel, conv_gain, ffn_gain)
    frames_part, kernel_part, conv_part, ffn_part = pull_back(
        (
            out_grad.astype(jnp.float32).reshape(utt_count, utt_len, feat_width),
            expert_back.reshape(utt_count, utt_len, feat_width),
        )
    )
    tap_count = kernel_part.shape[0]
    small_grads = butterfly_sum(
        jnp.concatenate([kernel_part, conv_part[None], ffn_part[None]], axis=0), ("dp", "expert")
    )
    kernel_grad = small_grads[:tap_count]
    gain_grads = small_grads[tap_count:]
    frames_grad = frames_part.reshape(frame_count, feat_width).astype(jnp.bfloat16)
    return (block_out, frames_grad, grad_in[None], grad_out[None], kernel_grad, gain_grads)


def solution(mesh):
    return jax.shard_map(
        shards,
        mesh=mesh,
        in_specs=(
            P(("dp", "expert"), None),
            P(("dp", "expert")),
            P(("dp", "expert"), None),
            P(),
            P(),
            P(),
            P("expert", None, None),
            P("expert", None, None),
            P(("dp", "expert"), None),
        ),
        out_specs=(
            P(("dp", "expert"), None),
            P(("dp", "expert"), None),
            P("expert", None, "dp"),
            P("expert", "dp", None),
            P(),
            P(),
        ),
        check_vma=False,
    )
```

```python
import jax
import jax.numpy as jnp
from jax import lax
from jax.sharding import PartitionSpec as P


def layer_norm(values, gain_vec):
    row_mean = jnp.mean(values, axis=-1, keepdims=True)
    centered = values - row_mean
    row_var = jnp.mean(centered * centered, axis=-1, keepdims=True)
    return centered * lax.rsqrt(row_var + 1e-05) * gain_vec


def conv_module(frames_f, live_mask, conv_kernel, conv_gain, ffn_gain):
    normed_conv = layer_norm(frames_f, conv_gain) * live_mask
    tap_count = conv_kernel.shape[0]
    half_span = (tap_count - 1) // 2
    utt_len = frames_f.shape[1]
    padded = jnp.pad(normed_conv, ((0, 0), (half_span, half_span), (0, 0)))
    conv_out = jnp.zeros_like(normed_conv)
    for tap_index in range(tap_count):
        conv_out = conv_out + conv_kernel[tap_index] * padded[:, tap_index : tap_index + utt_len]
    residual = frames_f + live_mask * jax.nn.silu(conv_out)
    return (residual, layer_norm(residual, ffn_gain))


def silu_slope(values):
    sig_val = jax.nn.sigmoid(values)
    return sig_val * (1.0 + values * (1.0 - sig_val))


def contract_rows(left_rows, right_rows):
    return lax.dot_general(
        left_rows, right_rows, (((0,), (0,)), ((), ())), preferred_element_type=jnp.float32
    )


def times_transpose(left_rows, matrix):
    return lax.dot_general(
        left_rows, matrix, (((1,), (1,)), ((), ())), preferred_element_type=jnp.float32
    )


def butterfly_sum(values, axis_names):
    for axis_name in axis_names:
        axis_len = lax.axis_size(axis_name)
        step = 1
        while step < axis_len:
            pairs = [(i, i ^ step) for i in range(axis_len)]
            values = values + lax.ppermute(values, axis_name, pairs)
            step *= 2
    return values


def shards(frames, lengths, expert_ids, conv_kernel, conv_gain, ffn_gain, w_in, w_out, out_grad):
    utt_count = lengths.shape[0]
    frame_count = frames.shape[0]
    utt_len = frame_count // utt_count
    feat_width = frames.shape[1]
    expert_count = lax.axis_size("expert")
    capacity = max(8, 8 * (9 * frame_count // (64 * expert_count)))
    slot_total = expert_count * capacity
    live_mask = (jnp.arange(utt_len, dtype=jnp.int32)[None, :] < lengths[:, None]).astype(
        jnp.float32
    )[:, :, None]
    live_flat = live_mask.reshape(frame_count) > 0.5
    target = jnp.where(live_flat, expert_ids[:, 0], expert_count)
    one_hot = (target[:, None] == jnp.arange(expert_count, dtype=jnp.int32)[None, :]).astype(
        jnp.int32
    )
    rank_in = jnp.sum((jnp.cumsum(one_hot, axis=0, dtype=jnp.int32) - 1) * one_hot, axis=1)
    dest_slot = jnp.where(live_flat, target * capacity + rank_in, slot_total)
    routed_grad = jnp.where(live_flat[:, None], out_grad, jnp.zeros_like(out_grad))
    send_grad = (
        jnp.zeros((slot_total, feat_width), jnp.bfloat16)
        .at[dest_slot]
        .set(routed_grad, mode="drop")
    )
    recv_grad = lax.all_to_all(
        send_grad.reshape(expert_count, capacity, feat_width),
        "expert",
        split_axis=0,
        concat_axis=0,
        tiled=True,
    )
    frames_f = frames.astype(jnp.float32).reshape(utt_count, utt_len, feat_width)
    residual, normed = conv_module(frames_f, live_mask, conv_kernel, conv_gain, ffn_gain)
    expert_in = normed.reshape(frame_count, feat_width).astype(jnp.bfloat16)
    send_in = (
        jnp.zeros((slot_total, feat_width), jnp.bfloat16).at[dest_slot].set(expert_in, mode="drop")
    )
    recv_grad, send_in = lax.optimization_barrier((recv_grad, send_in))
    recv_in = lax.all_to_all(
        send_in.reshape(expert_count, capacity, feat_width),
        "expert",
        split_axis=0,
        concat_axis=0,
        tiled=True,
    )
    routed_in = recv_in.reshape(slot_total, feat_width)
    grad_rows = recv_grad.reshape(slot_total, feat_width)
    weights_in = w_in[0]
    weights_out = w_out[0]
    pre_act = jnp.dot(routed_in, weights_in, preferred_element_type=jnp.float32)
    hidden = jax.nn.silu(pre_act).astype(jnp.bfloat16)
    full_out = contract_rows(hidden, grad_rows)
    full_out, pre_act, hidden, grad_rows, routed_in = lax.optimization_barrier(
        (full_out, pre_act, hidden, grad_rows, routed_in)
    )
    grad_out = lax.psum_scatter(full_out, "dp", scatter_dimension=0, tiled=True)
    out_rows = jnp.dot(hidden, weights_out, preferred_element_type=jnp.float32).astype(jnp.bfloat16)
    hidden_grad = times_transpose(grad_rows, weights_out)
    pre_grad = (hidden_grad * silu_slope(pre_act)).astype(jnp.bfloat16)
    full_in = contract_rows(routed_in, pre_grad)
    full_in, out_rows, pre_grad = lax.optimization_barrier((full_in, out_rows, pre_grad))
    grad_in = lax.psum_scatter(full_in, "dp", scatter_dimension=1, tiled=True)
    back_rows = times_transpose(pre_grad, weights_in).astype(jnp.bfloat16)
    ret_out, ret_back = (
        lax.all_to_all(
            out_rows.reshape(expert_count, capacity, feat_width),
            "expert",
            split_axis=0,
            concat_axis=0,
            tiled=True,
        ),
        lax.all_to_all(
            back_rows.reshape(expert_count, capacity, feat_width),
            "expert",
            split_axis=0,
            concat_axis=0,
            tiled=True,
        ),
    )
    safe_slot = jnp.minimum(dest_slot, slot_total - 1)
    zero_rows = jnp.zeros((frame_count, feat_width), jnp.float32)
    expert_out = jnp.where(
        live_flat[:, None],
        ret_out.reshape(slot_total, feat_width)[safe_slot].astype(jnp.float32),
        zero_rows,
    )
    expert_back = jnp.where(
        live_flat[:, None],
        ret_back.reshape(slot_total, feat_width)[safe_slot].astype(jnp.float32),
        zero_rows,
    )
    block_out = (residual.reshape(frame_count, feat_width) + expert_out).astype(jnp.bfloat16)

    def local_map(frames_in, kernel_in, gain_conv, gain_ffn):
        return conv_module(frames_in, live_mask, kernel_in, gain_conv, gain_ffn)

    unused_out, pull_back = jax.vjp(local_map, frames_f, conv_kernel, conv_gain, ffn_gain)
    frames_part, kernel_part, conv_part, ffn_part = pull_back(
        (
            out_grad.astype(jnp.float32).reshape(utt_count, utt_len, feat_width),
            expert_back.reshape(utt_count, utt_len, feat_width),
        )
    )
    tap_count = kernel_part.shape[0]
    small_grads = butterfly_sum(
        jnp.concatenate([kernel_part, conv_part[None], ffn_part[None]], axis=0), ("dp", "expert")
    )
    kernel_grad = small_grads[:tap_count]
    gain_grads = small_grads[tap_count:]
    frames_grad = frames_part.reshape(frame_count, feat_width).astype(jnp.bfloat16)
    return (block_out, frames_grad, grad_in[None], grad_out[None], kernel_grad, gain_grads)


def solution(mesh):
    return jax.shard_map(
        shards,
        mesh=mesh,
        in_specs=(
            P(("dp", "expert"), None),
            P(("dp", "expert")),
            P(("dp", "expert"), None),
            P(),
            P(),
            P(),
            P("expert", None, None),
            P("expert", None, None),
            P(("dp", "expert"), None),
        ),
        out_specs=(
            P(("dp", "expert"), None),
            P(("dp", "expert"), None),
            P("expert", None, "dp"),
            P("expert", "dp", None),
            P(),
            P(),
        ),
        check_vma=False,
    )
```

```python
import jax
import jax.numpy as jnp
from jax import lax
from jax.sharding import PartitionSpec as P


def layer_norm(values, gain_vec):
    row_mean = jnp.mean(values, axis=-1, keepdims=True)
    centered = values - row_mean
    row_var = jnp.mean(centered * centered, axis=-1, keepdims=True)
    return centered * lax.rsqrt(row_var + 1e-05) * gain_vec


def conv_module(frames_f, live_mask, conv_kernel, conv_gain, ffn_gain):
    normed_conv = layer_norm(frames_f, conv_gain) * live_mask
    tap_count = conv_kernel.shape[0]
    half_span = (tap_count - 1) // 2
    utt_len = frames_f.shape[1]
    padded = jnp.pad(normed_conv, ((0, 0), (half_span, half_span), (0, 0)))
    conv_out = jnp.zeros_like(normed_conv)
    for tap_index in range(tap_count):
        conv_out = conv_out + conv_kernel[tap_index] * padded[:, tap_index : tap_index + utt_len]
    residual = frames_f + live_mask * jax.nn.silu(conv_out)
    return (residual, layer_norm(residual, ffn_gain))


def silu_slope(values):
    sig_val = jax.nn.sigmoid(values)
    return sig_val * (1.0 + values * (1.0 - sig_val))


def contract_rows(left_rows, right_rows):
    return lax.dot_general(
        left_rows, right_rows, (((0,), (0,)), ((), ())), preferred_element_type=jnp.float32
    )


def times_transpose(left_rows, matrix):
    return lax.dot_general(
        left_rows, matrix, (((1,), (1,)), ((), ())), preferred_element_type=jnp.float32
    )


def butterfly_sum(values, axis_names):
    for axis_name in axis_names:
        axis_len = lax.axis_size(axis_name)
        step = 1
        while step < axis_len:
            pairs = [(i, i ^ step) for i in range(axis_len)]
            values = values + lax.ppermute(values, axis_name, pairs)
            step *= 2
    return values


def shards(frames, lengths, expert_ids, conv_kernel, conv_gain, ffn_gain, w_in, w_out, out_grad):
    utt_count = lengths.shape[0]
    frame_count = frames.shape[0]
    utt_len = frame_count // utt_count
    feat_width = frames.shape[1]
    expert_count = lax.axis_size("expert")
    capacity = max(8, 8 * (9 * frame_count // (64 * expert_count)))
    slot_total = expert_count * capacity
    live_mask = (jnp.arange(utt_len, dtype=jnp.int32)[None, :] < lengths[:, None]).astype(
        jnp.float32
    )[:, :, None]
    live_flat = live_mask.reshape(frame_count) > 0.5
    target = jnp.where(live_flat, expert_ids[:, 0], expert_count)
    one_hot = (target[:, None] == jnp.arange(expert_count, dtype=jnp.int32)[None, :]).astype(
        jnp.int32
    )
    rank_in = jnp.sum((jnp.cumsum(one_hot, axis=0, dtype=jnp.int32) - 1) * one_hot, axis=1)
    dest_slot = jnp.where(live_flat, target * capacity + rank_in, slot_total)
    routed_grad = jnp.where(live_flat[:, None], out_grad, jnp.zeros_like(out_grad))
    send_grad = (
        jnp.zeros((slot_total, feat_width), jnp.bfloat16)
        .at[dest_slot]
        .set(routed_grad, mode="drop")
    )
    recv_grad = lax.all_to_all(
        send_grad.reshape(expert_count, capacity, feat_width),
        "expert",
        split_axis=0,
        concat_axis=0,
        tiled=True,
    )
    frames_f = frames.astype(jnp.float32).reshape(utt_count, utt_len, feat_width)
    residual, normed = conv_module(frames_f, live_mask, conv_kernel, conv_gain, ffn_gain)
    expert_in = normed.reshape(frame_count, feat_width).astype(jnp.bfloat16)
    send_in = (
        jnp.zeros((slot_total, feat_width), jnp.bfloat16).at[dest_slot].set(expert_in, mode="drop")
    )
    recv_grad, send_in = lax.optimization_barrier((recv_grad, send_in))
    recv_in = lax.all_to_all(
        send_in.reshape(expert_count, capacity, feat_width),
        "expert",
        split_axis=0,
        concat_axis=0,
        tiled=True,
    )
    routed_in = recv_in.reshape(slot_total, feat_width)
    grad_rows = recv_grad.reshape(slot_total, feat_width)
    weights_in = w_in[0]
    weights_out = w_out[0]
    pre_act = jnp.dot(routed_in, weights_in, preferred_element_type=jnp.float32)
    hidden = jax.nn.silu(pre_act).astype(jnp.bfloat16)
    full_out = contract_rows(hidden, grad_rows)
    full_out, pre_act, hidden, grad_rows, routed_in = lax.optimization_barrier(
        (full_out, pre_act, hidden, grad_rows, routed_in)
    )
    grad_out = lax.psum_scatter(full_out, "dp", scatter_dimension=0, tiled=True)
    out_rows = jnp.dot(hidden, weights_out, preferred_element_type=jnp.float32).astype(jnp.bfloat16)
    hidden_grad = times_transpose(grad_rows, weights_out)
    pre_grad = (hidden_grad * silu_slope(pre_act)).astype(jnp.bfloat16)
    full_in = contract_rows(routed_in, pre_grad)
    full_in, out_rows, pre_grad = lax.optimization_barrier((full_in, out_rows, pre_grad))
    grad_in = lax.psum_scatter(full_in, "dp", scatter_dimension=1, tiled=True)
    back_rows = times_transpose(pre_grad, weights_in).astype(jnp.bfloat16)
    ret_out, ret_back = (
        lax.all_to_all(
            out_rows.reshape(expert_count, capacity, feat_width),
            "expert",
            split_axis=0,
            concat_axis=0,
            tiled=True,
        ),
        lax.all_to_all(
            back_rows.reshape(expert_count, capacity, feat_width),
            "expert",
            split_axis=0,
            concat_axis=0,
            tiled=True,
        ),
    )
    safe_slot = jnp.minimum(dest_slot, slot_total - 1)
    zero_rows = jnp.zeros((frame_count, feat_width), jnp.float32)
    expert_out = jnp.where(
        live_flat[:, None],
        ret_out.reshape(slot_total, feat_width)[safe_slot].astype(jnp.float32),
        zero_rows,
    )
    expert_back = jnp.where(
        live_flat[:, None],
        ret_back.reshape(slot_total, feat_width)[safe_slot].astype(jnp.float32),
        zero_rows,
    )
    block_out = (residual.reshape(frame_count, feat_width) + expert_out).astype(jnp.bfloat16)

    def local_map(frames_in, kernel_in, gain_conv, gain_ffn):
        return conv_module(frames_in, live_mask, kernel_in, gain_conv, gain_ffn)

    unused_out, pull_back = jax.vjp(local_map, frames_f, conv_kernel, conv_gain, ffn_gain)
    frames_part, kernel_part, conv_part, ffn_part = pull_back(
        (
            out_grad.astype(jnp.float32).reshape(utt_count, utt_len, feat_width),
            expert_back.reshape(utt_count, utt_len, feat_width),
        )
    )
    tap_count = kernel_part.shape[0]
    small_grads = butterfly_sum(
        jnp.concatenate([kernel_part, conv_part[None], ffn_part[None]], axis=0), ("expert", "dp")
    )
    kernel_grad = small_grads[:tap_count]
    gain_grads = small_grads[tap_count:]
    frames_grad = frames_part.reshape(frame_count, feat_width).astype(jnp.bfloat16)
    return (block_out, frames_grad, grad_in[None], grad_out[None], kernel_grad, gain_grads)


def solution(mesh):
    return jax.shard_map(
        shards,
        mesh=mesh,
        in_specs=(
            P(("dp", "expert"), None),
            P(("dp", "expert")),
            P(("dp", "expert"), None),
            P(),
            P(),
            P(),
            P("expert", None, None),
            P("expert", None, None),
            P(("dp", "expert"), None),
        ),
        out_specs=(
            P(("dp", "expert"), None),
            P(("dp", "expert"), None),
            P("expert", None, "dp"),
            P("expert", "dp", None),
            P(),
            P(),
        ),
        check_vma=False,
    )
```

```python
import jax
import jax.numpy as jnp
from jax import lax
from jax.sharding import PartitionSpec as P


def layer_norm(values, gain_vec):
    row_mean = jnp.mean(values, axis=-1, keepdims=True)
    centered = values - row_mean
    row_var = jnp.mean(centered * centered, axis=-1, keepdims=True)
    return centered * lax.rsqrt(row_var + 1e-05) * gain_vec


def conv_module(frames_f, live_mask, conv_kernel, conv_gain, ffn_gain):
    normed_conv = layer_norm(frames_f, conv_gain) * live_mask
    tap_count = conv_kernel.shape[0]
    half_span = (tap_count - 1) // 2
    utt_len = frames_f.shape[1]
    padded = jnp.pad(normed_conv, ((0, 0), (half_span, half_span), (0, 0)))
    conv_out = jnp.zeros_like(normed_conv)
    for tap_index in range(tap_count):
        conv_out = conv_out + conv_kernel[tap_index] * padded[:, tap_index : tap_index + utt_len]
    residual = frames_f + live_mask * jax.nn.silu(conv_out)
    return (residual, layer_norm(residual, ffn_gain))


def silu_slope(values):
    sig_val = jax.nn.sigmoid(values)
    return sig_val * (1.0 + values * (1.0 - sig_val))


def contract_rows(left_rows, right_rows):
    return lax.dot_general(
        left_rows, right_rows, (((0,), (0,)), ((), ())), preferred_element_type=jnp.float32
    )


def times_transpose(left_rows, matrix):
    return lax.dot_general(
        left_rows, matrix, (((1,), (1,)), ((), ())), preferred_element_type=jnp.float32
    )


def butterfly_sum(values, axis_names):
    for axis_name in axis_names:
        axis_len = lax.axis_size(axis_name)
        step = 1
        while step < axis_len:
            pairs = [(i, i ^ step) for i in range(axis_len)]
            values = values + lax.ppermute(values, axis_name, pairs)
            step *= 2
    return values


def shards(frames, lengths, expert_ids, conv_kernel, conv_gain, ffn_gain, w_in, w_out, out_grad):
    utt_count = lengths.shape[0]
    frame_count = frames.shape[0]
    utt_len = frame_count // utt_count
    feat_width = frames.shape[1]
    expert_count = lax.axis_size("expert")
    capacity = max(8, 8 * (9 * frame_count // (64 * expert_count)))
    slot_total = expert_count * capacity
    live_mask = (jnp.arange(utt_len, dtype=jnp.int32)[None, :] < lengths[:, None]).astype(
        jnp.float32
    )[:, :, None]
    live_flat = live_mask.reshape(frame_count) > 0.5
    target = jnp.where(live_flat, expert_ids[:, 0], expert_count)
    one_hot = (target[:, None] == jnp.arange(expert_count, dtype=jnp.int32)[None, :]).astype(
        jnp.int32
    )
    rank_in = jnp.sum((jnp.cumsum(one_hot, axis=0, dtype=jnp.int32) - 1) * one_hot, axis=1)
    dest_slot = jnp.where(live_flat, target * capacity + rank_in, slot_total)
    routed_grad = jnp.where(live_flat[:, None], out_grad, jnp.zeros_like(out_grad))
    send_grad = (
        jnp.zeros((slot_total, feat_width), jnp.bfloat16)
        .at[dest_slot]
        .set(routed_grad, mode="drop")
    )
    recv_grad = lax.all_to_all(
        send_grad.reshape(expert_count, capacity, feat_width),
        "expert",
        split_axis=0,
        concat_axis=0,
        tiled=True,
    )
    frames_f = frames.astype(jnp.float32).reshape(utt_count, utt_len, feat_width)
    residual, normed = conv_module(frames_f, live_mask, conv_kernel, conv_gain, ffn_gain)
    expert_in = normed.reshape(frame_count, feat_width).astype(jnp.bfloat16)
    send_in = (
        jnp.zeros((slot_total, feat_width), jnp.bfloat16).at[dest_slot].set(expert_in, mode="drop")
    )
    recv_grad, send_in = lax.optimization_barrier((recv_grad, send_in))
    recv_in = lax.all_to_all(
        send_in.reshape(expert_count, capacity, feat_width),
        "expert",
        split_axis=0,
        concat_axis=0,
        tiled=True,
    )
    routed_in = recv_in.reshape(slot_total, feat_width)
    grad_rows = recv_grad.reshape(slot_total, feat_width)
    weights_in = w_in[0]
    weights_out = w_out[0]
    pre_act = jnp.dot(routed_in, weights_in, preferred_element_type=jnp.float32)
    hidden = jax.nn.silu(pre_act).astype(jnp.bfloat16)
    full_out = contract_rows(hidden, grad_rows)
    full_out, pre_act, hidden, grad_rows, routed_in = lax.optimization_barrier(
        (full_out, pre_act, hidden, grad_rows, routed_in)
    )
    grad_out = lax.psum_scatter(full_out, "dp", scatter_dimension=0, tiled=True)
    out_rows = jnp.dot(hidden, weights_out, preferred_element_type=jnp.float32).astype(jnp.bfloat16)
    hidden_grad = times_transpose(grad_rows, weights_out)
    pre_grad = (hidden_grad * silu_slope(pre_act)).astype(jnp.bfloat16)
    full_in_t = contract_rows(pre_grad, routed_in)
    full_in_t, out_rows, pre_grad = lax.optimization_barrier((full_in_t, out_rows, pre_grad))
    grad_in = lax.psum_scatter(full_in_t, "dp", scatter_dimension=0, tiled=True).T
    back_rows = times_transpose(pre_grad, weights_in).astype(jnp.bfloat16)
    ret_out, ret_back = (
        lax.all_to_all(
            out_rows.reshape(expert_count, capacity, feat_width),
            "expert",
            split_axis=0,
            concat_axis=0,
            tiled=True,
        ),
        lax.all_to_all(
            back_rows.reshape(expert_count, capacity, feat_width),
            "expert",
            split_axis=0,
            concat_axis=0,
            tiled=True,
        ),
    )
    safe_slot = jnp.minimum(dest_slot, slot_total - 1)
    zero_rows = jnp.zeros((frame_count, feat_width), jnp.float32)
    expert_out = jnp.where(
        live_flat[:, None],
        ret_out.reshape(slot_total, feat_width)[safe_slot].astype(jnp.float32),
        zero_rows,
    )
    expert_back = jnp.where(
        live_flat[:, None],
        ret_back.reshape(slot_total, feat_width)[safe_slot].astype(jnp.float32),
        zero_rows,
    )
    block_out = (residual.reshape(frame_count, feat_width) + expert_out).astype(jnp.bfloat16)

    def local_map(frames_in, kernel_in, gain_conv, gain_ffn):
        return conv_module(frames_in, live_mask, kernel_in, gain_conv, gain_ffn)

    unused_out, pull_back = jax.vjp(local_map, frames_f, conv_kernel, conv_gain, ffn_gain)
    frames_part, kernel_part, conv_part, ffn_part = pull_back(
        (
            out_grad.astype(jnp.float32).reshape(utt_count, utt_len, feat_width),
            expert_back.reshape(utt_count, utt_len, feat_width),
        )
    )
    tap_count = kernel_part.shape[0]
    small_grads = butterfly_sum(
        jnp.concatenate([kernel_part, conv_part[None], ffn_part[None]], axis=0), ("expert", "dp")
    )
    kernel_grad = small_grads[:tap_count]
    gain_grads = small_grads[tap_count:]
    frames_grad = frames_part.reshape(frame_count, feat_width).astype(jnp.bfloat16)
    return (block_out, frames_grad, grad_in[None], grad_out[None], kernel_grad, gain_grads)


def solution(mesh):
    return jax.shard_map(
        shards,
        mesh=mesh,
        in_specs=(
            P(("dp", "expert"), None),
            P(("dp", "expert")),
            P(("dp", "expert"), None),
            P(),
            P(),
            P(),
            P("expert", None, None),
            P("expert", None, None),
            P(("dp", "expert"), None),
        ),
        out_specs=(
            P(("dp", "expert"), None),
            P(("dp", "expert"), None),
            P("expert", None, "dp"),
            P("expert", "dp", None),
            P(),
            P(),
        ),
        check_vma=False,
    )
```

```python
import jax
import jax.numpy as jnp
from jax import lax
from jax.sharding import PartitionSpec as P


def layer_norm(values, gain_vec):
    row_mean = jnp.mean(values, axis=-1, keepdims=True)
    centered = values - row_mean
    row_var = jnp.mean(centered * centered, axis=-1, keepdims=True)
    return centered * lax.rsqrt(row_var + 1e-05) * gain_vec


def conv_module(frames_f, live_mask, conv_kernel, conv_gain, ffn_gain):
    normed_conv = layer_norm(frames_f, conv_gain) * live_mask
    tap_count = conv_kernel.shape[0]
    half_span = (tap_count - 1) // 2
    utt_len = frames_f.shape[1]
    padded = jnp.pad(normed_conv, ((0, 0), (half_span, half_span), (0, 0)))
    conv_out = jnp.zeros_like(normed_conv)
    for tap_index in range(tap_count):
        conv_out = conv_out + conv_kernel[tap_index] * padded[:, tap_index : tap_index + utt_len]
    residual = frames_f + live_mask * jax.nn.silu(conv_out)
    return (residual, layer_norm(residual, ffn_gain))


def silu_slope(values):
    sig_val = jax.nn.sigmoid(values)
    return sig_val * (1.0 + values * (1.0 - sig_val))


def contract_rows(left_rows, right_rows):
    return lax.dot_general(
        left_rows, right_rows, (((0,), (0,)), ((), ())), preferred_element_type=jnp.float32
    )


def times_transpose(left_rows, matrix):
    return lax.dot_general(
        left_rows, matrix, (((1,), (1,)), ((), ())), preferred_element_type=jnp.float32
    )


def butterfly_sum(values, axis_names):
    for axis_name in axis_names:
        axis_len = lax.axis_size(axis_name)
        step = 1
        while step < axis_len:
            pairs = [(i, i ^ step) for i in range(axis_len)]
            values = values + lax.ppermute(values, axis_name, pairs)
            step *= 2
    return values


def shards(frames, lengths, expert_ids, conv_kernel, conv_gain, ffn_gain, w_in, w_out, out_grad):
    utt_count = lengths.shape[0]
    frame_count = frames.shape[0]
    utt_len = frame_count // utt_count
    feat_width = frames.shape[1]
    expert_count = lax.axis_size("expert")
    capacity = max(8, 8 * (9 * frame_count // (64 * expert_count)))
    slot_total = expert_count * capacity
    live_mask = (jnp.arange(utt_len, dtype=jnp.int32)[None, :] < lengths[:, None]).astype(
        jnp.float32
    )[:, :, None]
    live_flat = live_mask.reshape(frame_count) > 0.5
    target = jnp.where(live_flat, expert_ids[:, 0], expert_count)
    one_hot = (target[:, None] == jnp.arange(expert_count, dtype=jnp.int32)[None, :]).astype(
        jnp.int32
    )
    rank_in = jnp.sum((jnp.cumsum(one_hot, axis=0, dtype=jnp.int32) - 1) * one_hot, axis=1)
    dest_slot = jnp.where(live_flat, target * capacity + rank_in, slot_total)
    routed_grad = jnp.where(live_flat[:, None], out_grad, jnp.zeros_like(out_grad))
    send_grad = (
        jnp.zeros((slot_total, feat_width), jnp.bfloat16)
        .at[dest_slot]
        .set(routed_grad, mode="drop")
    )
    recv_grad = lax.all_to_all(
        send_grad.reshape(expert_count, capacity, feat_width),
        "expert",
        split_axis=0,
        concat_axis=0,
        tiled=True,
    )
    frames_f = frames.astype(jnp.float32).reshape(utt_count, utt_len, feat_width)
    residual, normed = conv_module(frames_f, live_mask, conv_kernel, conv_gain, ffn_gain)
    expert_in = normed.reshape(frame_count, feat_width).astype(jnp.bfloat16)
    send_in = (
        jnp.zeros((slot_total, feat_width), jnp.bfloat16).at[dest_slot].set(expert_in, mode="drop")
    )
    recv_grad, send_in = lax.optimization_barrier((recv_grad, send_in))
    recv_in = lax.all_to_all(
        send_in.reshape(expert_count, capacity, feat_width),
        "expert",
        split_axis=0,
        concat_axis=0,
        tiled=True,
    )
    routed_in = recv_in.reshape(slot_total, feat_width)
    grad_rows = recv_grad.reshape(slot_total, feat_width)
    weights_in = w_in[0]
    weights_out = w_out[0]
    ff_width = weights_in.shape[1]
    dp_count = lax.axis_size("dp")
    piece = ff_width // (2 * dp_count)
    w_in_halves = [
        weights_in.reshape(feat_width, dp_count, 2, piece)[:, :, part].reshape(
            feat_width, ff_width // 2
        )
        for part in range(2)
    ]
    w_out_halves = [
        weights_out.reshape(dp_count, 2, piece, feat_width)[:, part].reshape(
            ff_width // 2, feat_width
        )
        for part in range(2)
    ]
    pre_first = jnp.dot(routed_in, w_in_halves[0], preferred_element_type=jnp.float32)
    hidden_first = jax.nn.silu(pre_first).astype(jnp.bfloat16)
    out_first = contract_rows(hidden_first, grad_rows)
    out_first, pre_first, hidden_first, grad_rows, routed_in = lax.optimization_barrier(
        (out_first, pre_first, hidden_first, grad_rows, routed_in)
    )
    grad_out_first = lax.psum_scatter(out_first, "dp", scatter_dimension=0, tiled=True)
    pre_second = jnp.dot(routed_in, w_in_halves[1], preferred_element_type=jnp.float32)
    hidden_second = jax.nn.silu(pre_second).astype(jnp.bfloat16)
    out_second = contract_rows(hidden_second, grad_rows)
    out_second, pre_second, hidden_second, grad_rows, routed_in = lax.optimization_barrier(
        (out_second, pre_second, hidden_second, grad_rows, routed_in)
    )
    grad_out_second = lax.psum_scatter(out_second, "dp", scatter_dimension=0, tiled=True)
    grad_out = jnp.concatenate([grad_out_first, grad_out_second], axis=0)
    pre_act = [pre_first, pre_second]
    hidden = [hidden_first, hidden_second]
    out_rows = (
        jnp.dot(hidden[0], w_out_halves[0], preferred_element_type=jnp.float32)
        + jnp.dot(hidden[1], w_out_halves[1], preferred_element_type=jnp.float32)
    ).astype(jnp.bfloat16)
    pre_grad = [
        (times_transpose(grad_rows, w_out_halves[part]) * silu_slope(pre_act[part])).astype(
            jnp.bfloat16
        )
        for part in range(2)
    ]
    full_in = jnp.stack(
        [
            contract_rows(routed_in, pre_grad[part]).reshape(feat_width, dp_count, piece)
            for part in range(2)
        ],
        axis=2,
    ).reshape(feat_width, ff_width)
    full_in, out_rows, pre_first_grad, pre_second_grad = lax.optimization_barrier(
        (full_in, out_rows, pre_grad[0], pre_grad[1])
    )
    grad_in = lax.psum_scatter(full_in, "dp", scatter_dimension=1, tiled=True)
    back_rows = (
        times_transpose(pre_first_grad, w_in_halves[0])
        + times_transpose(pre_second_grad, w_in_halves[1])
    ).astype(jnp.bfloat16)
    ret_out, ret_back = (
        lax.all_to_all(
            out_rows.reshape(expert_count, capacity, feat_width),
            "expert",
            split_axis=0,
            concat_axis=0,
            tiled=True,
        ),
        lax.all_to_all(
            back_rows.reshape(expert_count, capacity, feat_width),
            "expert",
            split_axis=0,
            concat_axis=0,
            tiled=True,
        ),
    )
    safe_slot = jnp.minimum(dest_slot, slot_total - 1)
    zero_rows = jnp.zeros((frame_count, feat_width), jnp.float32)
    expert_out = jnp.where(
        live_flat[:, None],
        ret_out.reshape(slot_total, feat_width)[safe_slot].astype(jnp.float32),
        zero_rows,
    )
    expert_back = jnp.where(
        live_flat[:, None],
        ret_back.reshape(slot_total, feat_width)[safe_slot].astype(jnp.float32),
        zero_rows,
    )
    block_out = (residual.reshape(frame_count, feat_width) + expert_out).astype(jnp.bfloat16)

    def local_map(frames_in, kernel_in, gain_conv, gain_ffn):
        return conv_module(frames_in, live_mask, kernel_in, gain_conv, gain_ffn)

    unused_out, pull_back = jax.vjp(local_map, frames_f, conv_kernel, conv_gain, ffn_gain)
    frames_part, kernel_part, conv_part, ffn_part = pull_back(
        (
            out_grad.astype(jnp.float32).reshape(utt_count, utt_len, feat_width),
            expert_back.reshape(utt_count, utt_len, feat_width),
        )
    )
    tap_count = kernel_part.shape[0]
    small_grads = butterfly_sum(
        jnp.concatenate([kernel_part, conv_part[None], ffn_part[None]], axis=0), ("expert", "dp")
    )
    kernel_grad = small_grads[:tap_count]
    gain_grads = small_grads[tap_count:]
    frames_grad = frames_part.reshape(frame_count, feat_width).astype(jnp.bfloat16)
    return (block_out, frames_grad, grad_in[None], grad_out[None], kernel_grad, gain_grads)


def solution(mesh):
    return jax.shard_map(
        shards,
        mesh=mesh,
        in_specs=(
            P(("dp", "expert"), None),
            P(("dp", "expert")),
            P(("dp", "expert"), None),
            P(),
            P(),
            P(),
            P("expert", None, None),
            P("expert", None, None),
            P(("dp", "expert"), None),
        ),
        out_specs=(
            P(("dp", "expert"), None),
            P(("dp", "expert"), None),
            P("expert", None, "dp"),
            P("expert", "dp", None),
            P(),
            P(),
        ),
        check_vma=False,
    )
```

```python
import jax
import jax.numpy as jnp
from jax import lax
from jax.sharding import PartitionSpec as P


def layer_norm(values, gain_vec):
    row_mean = jnp.mean(values, axis=-1, keepdims=True)
    centered = values - row_mean
    row_var = jnp.mean(centered * centered, axis=-1, keepdims=True)
    return centered * lax.rsqrt(row_var + 1e-05) * gain_vec


def conv_module(frames_f, live_mask, conv_kernel, conv_gain, ffn_gain):
    normed_conv = layer_norm(frames_f, conv_gain) * live_mask
    tap_count = conv_kernel.shape[0]
    half_span = (tap_count - 1) // 2
    utt_len = frames_f.shape[1]
    padded = jnp.pad(normed_conv, ((0, 0), (half_span, half_span), (0, 0)))
    conv_out = jnp.zeros_like(normed_conv)
    for tap_index in range(tap_count):
        conv_out = conv_out + conv_kernel[tap_index] * padded[:, tap_index : tap_index + utt_len]
    residual = frames_f + live_mask * jax.nn.silu(conv_out)
    return (residual, layer_norm(residual, ffn_gain))


def silu_slope(values):
    sig_val = jax.nn.sigmoid(values)
    return sig_val * (1.0 + values * (1.0 - sig_val))


def contract_rows(left_rows, right_rows):
    return lax.dot_general(
        left_rows, right_rows, (((0,), (0,)), ((), ())), preferred_element_type=jnp.float32
    )


def times_transpose(left_rows, matrix):
    return lax.dot_general(
        left_rows, matrix, (((1,), (1,)), ((), ())), preferred_element_type=jnp.float32
    )


def butterfly_sum(values, axis_names):
    for axis_name in axis_names:
        axis_len = lax.axis_size(axis_name)
        step = 1
        while step < axis_len:
            pairs = [(i, i ^ step) for i in range(axis_len)]
            values = values + lax.ppermute(values, axis_name, pairs)
            step *= 2
    return values


def shards(frames, lengths, expert_ids, conv_kernel, conv_gain, ffn_gain, w_in, w_out, out_grad):
    utt_count = lengths.shape[0]
    frame_count = frames.shape[0]
    utt_len = frame_count // utt_count
    feat_width = frames.shape[1]
    expert_count = lax.axis_size("expert")
    capacity = max(8, 8 * (9 * frame_count // (64 * expert_count)))
    slot_total = expert_count * capacity
    live_mask = (jnp.arange(utt_len, dtype=jnp.int32)[None, :] < lengths[:, None]).astype(
        jnp.float32
    )[:, :, None]
    live_flat = live_mask.reshape(frame_count) > 0.5
    target = jnp.where(live_flat, expert_ids[:, 0], expert_count)
    one_hot = (target[:, None] == jnp.arange(expert_count, dtype=jnp.int32)[None, :]).astype(
        jnp.int32
    )
    rank_in = jnp.sum((jnp.cumsum(one_hot, axis=0, dtype=jnp.int32) - 1) * one_hot, axis=1)
    dest_slot = jnp.where(live_flat, target * capacity + rank_in, slot_total)
    routed_grad = jnp.where(live_flat[:, None], out_grad, jnp.zeros_like(out_grad))
    slot_src = (
        jnp.full((slot_total,), frame_count, jnp.int32)
        .at[dest_slot]
        .set(jnp.arange(frame_count, dtype=jnp.int32), mode="drop")
    )
    slot_used = (slot_src < frame_count)[:, None]
    slot_row = jnp.minimum(slot_src, frame_count - 1)
    send_grad = jnp.where(slot_used, routed_grad[slot_row], jnp.zeros((), jnp.bfloat16))
    recv_grad = lax.all_to_all(
        send_grad.reshape(expert_count, capacity, feat_width),
        "expert",
        split_axis=0,
        concat_axis=0,
        tiled=True,
    )
    frames_f = frames.astype(jnp.float32).reshape(utt_count, utt_len, feat_width)
    residual, normed = conv_module(frames_f, live_mask, conv_kernel, conv_gain, ffn_gain)
    expert_in = normed.reshape(frame_count, feat_width).astype(jnp.bfloat16)
    send_in = jnp.where(slot_used, expert_in[slot_row], jnp.zeros((), jnp.bfloat16))
    recv_grad, send_in = lax.optimization_barrier((recv_grad, send_in))
    recv_in = lax.all_to_all(
        send_in.reshape(expert_count, capacity, feat_width),
        "expert",
        split_axis=0,
        concat_axis=0,
        tiled=True,
    )
    routed_in = recv_in.reshape(slot_total, feat_width)
    grad_rows = recv_grad.reshape(slot_total, feat_width)
    weights_in = w_in[0]
    weights_out = w_out[0]
    pre_act = jnp.dot(routed_in, weights_in, preferred_element_type=jnp.float32)
    hidden = jax.nn.silu(pre_act).astype(jnp.bfloat16)
    full_out = contract_rows(hidden, grad_rows)
    full_out, pre_act, hidden, grad_rows, routed_in = lax.optimization_barrier(
        (full_out, pre_act, hidden, grad_rows, routed_in)
    )
    grad_out = lax.psum_scatter(full_out, "dp", scatter_dimension=0, tiled=True)
    out_rows = jnp.dot(hidden, weights_out, preferred_element_type=jnp.float32).astype(jnp.bfloat16)
    hidden_grad = times_transpose(grad_rows, weights_out)
    pre_grad = (hidden_grad * silu_slope(pre_act)).astype(jnp.bfloat16)
    full_in = contract_rows(routed_in, pre_grad)
    full_in, out_rows, pre_grad = lax.optimization_barrier((full_in, out_rows, pre_grad))
    grad_in = lax.psum_scatter(full_in, "dp", scatter_dimension=1, tiled=True)
    back_rows = times_transpose(pre_grad, weights_in).astype(jnp.bfloat16)
    ret_out, ret_back = (
        lax.all_to_all(
            out_rows.reshape(expert_count, capacity, feat_width),
            "expert",
            split_axis=0,
            concat_axis=0,
            tiled=True,
        ),
        lax.all_to_all(
            back_rows.reshape(expert_count, capacity, feat_width),
            "expert",
            split_axis=0,
            concat_axis=0,
            tiled=True,
        ),
    )
    safe_slot = jnp.minimum(dest_slot, slot_total - 1)
    zero_rows = jnp.zeros((frame_count, feat_width), jnp.float32)
    expert_out = jnp.where(
        live_flat[:, None],
        ret_out.reshape(slot_total, feat_width)[safe_slot].astype(jnp.float32),
        zero_rows,
    )
    expert_back = jnp.where(
        live_flat[:, None],
        ret_back.reshape(slot_total, feat_width)[safe_slot].astype(jnp.float32),
        zero_rows,
    )
    block_out = (residual.reshape(frame_count, feat_width) + expert_out).astype(jnp.bfloat16)

    def local_map(frames_in, kernel_in, gain_conv, gain_ffn):
        return conv_module(frames_in, live_mask, kernel_in, gain_conv, gain_ffn)

    unused_out, pull_back = jax.vjp(local_map, frames_f, conv_kernel, conv_gain, ffn_gain)
    frames_part, kernel_part, conv_part, ffn_part = pull_back(
        (
            out_grad.astype(jnp.float32).reshape(utt_count, utt_len, feat_width),
            expert_back.reshape(utt_count, utt_len, feat_width),
        )
    )
    tap_count = kernel_part.shape[0]
    small_grads = butterfly_sum(
        jnp.concatenate([kernel_part, conv_part[None], ffn_part[None]], axis=0), ("expert", "dp")
    )
    kernel_grad = small_grads[:tap_count]
    gain_grads = small_grads[tap_count:]
    frames_grad = frames_part.reshape(frame_count, feat_width).astype(jnp.bfloat16)
    return (block_out, frames_grad, grad_in[None], grad_out[None], kernel_grad, gain_grads)


def solution(mesh):
    return jax.shard_map(
        shards,
        mesh=mesh,
        in_specs=(
            P(("dp", "expert"), None),
            P(("dp", "expert")),
            P(("dp", "expert"), None),
            P(),
            P(),
            P(),
            P("expert", None, None),
            P("expert", None, None),
            P(("dp", "expert"), None),
        ),
        out_specs=(
            P(("dp", "expert"), None),
            P(("dp", "expert"), None),
            P("expert", None, "dp"),
            P("expert", "dp", None),
            P(),
            P(),
        ),
        check_vma=False,
    )
```
